256 devices in a mesh: dp: 4 (over y), section: 16 (over z, x_lo), tensor: 4 (over x_hi, core).
Axes of the slice: x: 4 (x_hi: 2, x_lo: 2; x = x_hi * 2 + x_lo), y: 4, z: 8, core: 2. Of those that a mesh axis runs over, the one named last changes fastest.
Arguments:
- saved_input: bfloat16 [16, 2, 512, 8192], P('section', None, ('dp', 'tensor')), may hold values from -6 to 6
- kv_grad: bfloat16 [16, 2, 512, 2048], P('section', None, 'dp', 'tensor'), may hold values from -1.5 to 1.5
- kv_weight: bfloat16 [16, 8192, 2048], P('section', 'dp', 'tensor'), may hold values from -0.0625 to 0.0625
- norm_gain: bfloat16 [16, 8192], P('section'), may hold values from 0.5 to 1.5
- top_grad: bfloat16 [2, 512, 8192], P(None, ('dp', 'tensor')), may hold values from -1.5 to 1.5
- noise_salt: int32 [1], replicated, may hold values from 0 to 1073741823
- step_counter: int32 [1], replicated, may hold values from 0 to 999999
Outputs:
- input_grads: bfloat16 [16, 2, 512, 8192], P('section', None, ('dp', 'tensor'))
- weight_grads: float32 [16, 8192, 2048], P('section', 'dp', 'tensor')
The draws below stay inside these ranges and needn't reach their ends.
All inputs are finite; a program needn't handle non-finite values.
Results may differ from the reference program's by a relative error of at most 0.012.
Values may be sent and summed in bfloat16 or wider, within the bound.
No kernel may reach another device: no remote copies, remote signals or barrier semaphores. Data moves between devices by JAX's collectives and lax.ppermute only.
A program may use at most 128 MiB of HBM per device.

```python
import jax
import jax.numpy as jnp
from jax import lax

D = 8192
MB = 2
TOK_DEV = 32
KVW = 2048
LAYERS = 16
TOKENS = 512
N_DP = 4
N_TENSOR = 4


def block_levels(own_key, dims, split, low, high):
    def one(axis_at, shards_of):
        heights = jax.random.uniform(jax.random.fold_in(jax.random.fold_in(own_key, 6), axis_at), (shards_of,), jnp.float32, low / len(split), high / len(split))
        return jnp.repeat(jnp.exp(heights), dims[axis_at] // shards_of).reshape((-1,) + (1,) * (len(dims) - axis_at - 1))

    level = one(*split[0])
    for cut in split[1:]:
        level = level * one(*cut)
    return level


def bell_draw(rng, shape, width, bound, shards=(), held_as=jnp.bfloat16):
    level = block_levels(rng, shape, shards, -0.22, 0.18) if shards else 1.0
    entries = jax.random.normal(rng, shape, jnp.float32) * width * level
    return jnp.minimum(jnp.maximum(entries, -bound), bound).astype(held_as)


def setup_inputs(seed: int = 0) -> dict:
    keys = jax.random.split(jax.random.key(seed), 8)
    return {
        "saved_input": bell_draw(keys[0], (LAYERS, MB, TOKENS, D), 1.0, 6.0, ((0, 16), (2, 16))),
        "kv_grad": bell_draw(keys[1], (LAYERS, MB, TOKENS, KVW), 0.25, 1.5, ((0, 16), (2, 4), (3, 4))),
        "kv_weight": bell_draw(keys[2], (LAYERS, D, KVW), D ** -0.5, 0.0625, ((0, 16), (1, 4), (2, 4))),
        "norm_gain": jnp.clip(1.0 + 0.1 * jax.random.normal(keys[3], (LAYERS, D), jnp.float32), 0.5, 1.5).astype(jnp.bfloat16),
        "top_grad": bell_draw(keys[4], (MB, TOKENS, D), 0.25, 1.5, ((1, 16),)),
        "noise_salt": jax.random.randint(keys[5], (1,), 0, 1073741824).astype(jnp.int32),
        "step_counter": jax.random.randint(keys[6], (1,), 0, 1000000).astype(jnp.int32),
    }


def mix_bits(salt, counter, layer, group, index):
    h = index * jnp.int32(-1640531535) + salt * jnp.int32(374761393) + counter * jnp.int32(668265263)
    h = h + layer * jnp.int32(-1028477379) + group * jnp.int32(1274126177)
    h = h ^ lax.shift_right_logical(h, jnp.int32(16))
    h = h * jnp.int32(2146121005)
    h = h ^ lax.shift_right_logical(h, jnp.int32(15))
    h = h * jnp.int32(-2073254261)
    h = h ^ lax.shift_right_logical(h, jnp.int32(16))
    return lax.shift_right_logical(h, jnp.int32(8)).astype(jnp.float32) * (1.0 / 16777216.0)

def dither(term, salt, counter, layer, group, index):
    noise = mix_bits(salt, counter, layer, group, index)
    moved = term * (1.0 + (noise - 0.5) * 0.5)
    return lax.optimization_barrier(moved.astype(jnp.bfloat16)).astype(jnp.float32)

def reference(saved_input, kv_grad, kv_weight, norm_gain, top_grad, noise_salt, step_counter):
    salt = noise_salt[0]
    counter = step_counter[0]
    width_t = KVW // N_TENSOR
    rows_group = TOK_DEV * N_TENSOR
    top = top_grad.astype(jnp.float32)
    index = jnp.arange(D, dtype=jnp.int32)[:, None] * jnp.int32(KVW) + jnp.arange(KVW, dtype=jnp.int32)[None, :]

    def layer_step(acc, item):
        layer, inputs, cotan, weight, gain = item
        input_float = inputs.astype(jnp.float32)
        inverse_scale = lax.rsqrt(lax.optimization_barrier(jnp.mean(input_float * input_float, axis=-1, keepdims=True)) + 1e-05)
        centered_input = input_float * inverse_scale
        gain_float = gain.astype(jnp.float32)
        normed_values = (centered_input * gain_float).astype(jnp.bfloat16)
        cotanf = cotan.astype(jnp.float32)
        weightf = weight.astype(jnp.float32)
        normed_grad = jnp.zeros((MB, TOKENS, D), jnp.float32)
        for group_t in range(N_TENSOR):
            cols = slice(group_t * width_t, (group_t + 1) * width_t)
            part = jnp.einsum('mtk,dk->mtd', cotanf[:, :, cols], weightf[:, cols])
            normed_grad = normed_grad + part.astype(jnp.bfloat16).astype(jnp.float32)
        hidden_gradient = normed_grad * gain_float
        branch_path = inverse_scale * (hidden_gradient - centered_input * lax.optimization_barrier(jnp.mean(hidden_gradient * centered_input, axis=-1, keepdims=True)))
        acc = acc + branch_path
        grad_in = (top + acc).astype(jnp.bfloat16)
        normedf = normed_values.astype(jnp.float32)
        wsum = jnp.zeros((D, KVW), jnp.float32)
        for group_p in range(N_DP):
            rows = slice(group_p * rows_group, (group_p + 1) * rows_group)
            partial_p = jnp.einsum('mtd,mtk->dk', normedf[:, rows], cotanf[:, rows])
            wsum = wsum + dither(partial_p, salt, counter, layer, jnp.int32(group_p), index)
        return (acc, (grad_in, wsum))
    start = jnp.zeros((MB, TOKENS, D), jnp.float32)
    layers = jnp.arange(LAYERS, dtype=jnp.int32)
    _, outs = lax.scan(layer_step, start, (layers, saved_input, kv_grad, kv_weight, norm_gain), reverse=True)
    return (outs[0], outs[1])
```

```python
import jax
import jax.numpy as jnp
from jax import lax
from jax.sharding import PartitionSpec as P


def mix_bits(salt, counter, layer, group, index):
    h = (
        index * jnp.int32(-1640531535)
        + salt * jnp.int32(374761393)
        + counter * jnp.int32(668265263)
    )
    h = h + layer * jnp.int32(-1028477379) + group * jnp.int32(1274126177)
    h = h ^ lax.shift_right_logical(h, jnp.int32(16))
    h = h * jnp.int32(2146121005)
    h = h ^ lax.shift_right_logical(h, jnp.int32(15))
    h = h * jnp.int32(-2073254261)
    h = h ^ lax.shift_right_logical(h, jnp.int32(16))
    return lax.shift_right_logical(h, jnp.int32(8)).astype(jnp.float32) * (1.0 / 16777216.0)


def dither(term, salt, counter, layer, group, index):
    noise = mix_bits(salt, counter, layer, group, index)
    moved = term * (1.0 + (noise - 0.5) * 0.5)
    return lax.optimization_barrier(moved.astype(jnp.bfloat16)).astype(jnp.float32)


def later_sum(branch_path):
    n_sec = lax.axis_size("section")
    m, t, d = branch_path.shape
    chunks = lax.all_to_all(
        branch_path.astype(jnp.bfloat16)[None], "section", 3, 0, tiled=True
    ).astype(jnp.float32)
    acc = jnp.zeros(chunks.shape[1:], jnp.float32)
    outs = [None] * n_sec
    for s in range(n_sec - 1, -1, -1):
        outs[s] = acc
        acc = acc + chunks[s]
    stacked = jnp.stack(outs).astype(jnp.bfloat16)
    back = lax.all_to_all(stacked, "section", 0, 3, tiled=True)
    return back[0].astype(jnp.float32)


def shards(saved_input, kv_grad, kv_weight, norm_gain, top_grad, noise_salt, step_counter):
    salt = noise_salt[0]
    counter = step_counter[0]
    layer = lax.axis_index("section")
    n_dp = lax.axis_size("dp")
    n_t = lax.axis_size("tensor")
    my_p = lax.axis_index("dp")
    my_t = lax.axis_index("tensor")
    cotan = kv_grad[0]
    weight = kv_weight[0]
    rows_p, width_t = weight.shape
    total_cols = width_t * n_t
    mb, tok_dev, d_model = saved_input.shape[1:]

    input_float = saved_input[0].astype(jnp.float32)
    inverse_scale = lax.rsqrt(jnp.mean(input_float * input_float, axis=-1, keepdims=True) + 1e-05)
    centered_input = input_float * inverse_scale
    gain_float = norm_gain[0].astype(jnp.float32)
    normed_values = (centered_input * gain_float).astype(jnp.bfloat16)

    cotan_all = lax.all_gather(cotan, "dp", axis=1, tiled=True)
    part = jnp.einsum(
        "mtk,dk->mtd", cotan_all, weight, preferred_element_type=jnp.float32
    ).astype(jnp.bfloat16)
    part = part.reshape(mb, n_dp * n_t, tok_dev, rows_p).transpose(1, 0, 2, 3)
    got = lax.all_to_all(part, ("dp", "tensor"), 0, 0, tiled=True)
    got = got.reshape(n_dp, n_t, mb, tok_dev, rows_p).astype(jnp.float32)
    normed_grad = got[:, 0]
    for t in range(1, n_t):
        normed_grad = normed_grad + got[:, t]
    normed_grad = normed_grad.transpose(1, 2, 0, 3).reshape(mb, tok_dev, d_model)

    hidden_gradient = normed_grad * gain_float
    branch_path = inverse_scale * (
        hidden_gradient
        - centered_input * jnp.mean(hidden_gradient * centered_input, axis=-1, keepdims=True)
    )
    later = later_sum(branch_path)
    grad_in = (top_grad.astype(jnp.float32) + branch_path + later).astype(jnp.bfloat16)

    nrm = normed_values.reshape(mb, tok_dev, n_dp, rows_p).transpose(2, 0, 1, 3)
    nrm = lax.all_to_all(nrm, "dp", 0, 0, tiled=True)
    nrm = lax.all_gather(nrm, "tensor", axis=0, tiled=False)
    cot = cotan_all.reshape(mb, n_dp, n_t, tok_dev, width_t)
    terms = jnp.einsum("tpmid,mptik->pdk", nrm, cot, preferred_element_type=jnp.float32)

    row_ids = my_p * jnp.int32(rows_p) + jnp.arange(rows_p, dtype=jnp.int32)
    index = (
        row_ids[:, None] * jnp.int32(total_cols)
        + my_t * jnp.int32(width_t)
        + jnp.arange(width_t, dtype=jnp.int32)[None, :]
    )
    wsum = jnp.zeros((rows_p, width_t), jnp.float32)
    for g in range(n_dp):
        wsum = wsum + dither(terms[g], salt, counter, layer, jnp.int32(g), index)
    return (grad_in[None], wsum[None])


def solution(mesh):
    placed = (
        P("section", None, ("dp", "tensor"), None),
        P("section", None, "dp", "tensor"),
        P("section", "dp", "tensor"),
        P("section", None),
        P(None, ("dp", "tensor"), None),
        P(),
        P(),
    )
    return jax.shard_map(
        shards,
        mesh=mesh,
        in_specs=placed,
        out_specs=(P("section", None, ("dp", "tensor"), None), P("section", "dp", "tensor")),
        check_vma=False,
    )
```

```python
import jax
import jax.numpy as jnp
from jax import lax
from jax.sharding import PartitionSpec as P


def mix_bits(salt, counter, layer, group, index):
    h = (
        index * jnp.int32(-1640531535)
        + salt * jnp.int32(374761393)
        + counter * jnp.int32(668265263)
    )
    h = h + layer * jnp.int32(-1028477379) + group * jnp.int32(1274126177)
    h = h ^ lax.shift_right_logical(h, jnp.int32(16))
    h = h * jnp.int32(2146121005)
    h = h ^ lax.shift_right_logical(h, jnp.int32(15))
    h = h * jnp.int32(-2073254261)
    h = h ^ lax.shift_right_logical(h, jnp.int32(16))
    return lax.shift_right_logical(h, jnp.int32(8)).astype(jnp.float32) * (1.0 / 16777216.0)


def dither(term, salt, counter, layer, group, index):
    noise = mix_bits(salt, counter, layer, group, index)
    moved = term * (1.0 + (noise - 0.5) * 0.5)
    return lax.optimization_barrier(moved.astype(jnp.bfloat16)).astype(jnp.float32)


def later_sum(branch_path):
    n_sec = lax.axis_size("section")
    m, t, d = branch_path.shape
    rt = t // 8
    half = n_sec // (m * rt)
    w = d // half
    chunks = branch_path.astype(jnp.bfloat16).reshape(m, rt, 8, half, w)
    chunks = chunks.transpose(0, 1, 3, 2, 4).reshape(n_sec, 8, w)
    got = lax.all_to_all(chunks, "section", 0, 0, tiled=True)
    src = jnp.arange(n_sec, dtype=jnp.int32)
    upper = (src[None, :] > src[:, None]).astype(jnp.bfloat16)
    suffix = jnp.einsum(
        "st,tx->sx", upper, got.reshape(n_sec, -1), preferred_element_type=jnp.float32
    )
    back = lax.all_to_all(
        suffix.astype(jnp.bfloat16).reshape(n_sec, 8, w), "section", 0, 0, tiled=True
    )
    back = back.reshape(m, rt, half, 8, w).transpose(0, 1, 3, 2, 4)
    return back.reshape(m, t, d).astype(jnp.float32)


def body(saved_input, kv_grad, kv_weight, norm_gain, top_grad, noise_salt, step_counter):
    salt = noise_salt[0]
    counter = step_counter[0]
    layer = lax.axis_index("section")
    n_dp = lax.axis_size("dp")
    n_t = lax.axis_size("tensor")
    my_p = lax.axis_index("dp")
    my_t = lax.axis_index("tensor")
    cotan = kv_grad[0]
    weight = kv_weight[0]
    rows_p, width_t = weight.shape
    total_cols = width_t * n_t
    mb, tok_dev, d_model = saved_input.shape[1:]

    input_float = saved_input[0].astype(jnp.float32)
    inverse_scale = lax.rsqrt(jnp.mean(input_float * input_float, axis=-1, keepdims=True) + 1e-05)
    centered_input = input_float * inverse_scale
    gain_float = norm_gain[0].astype(jnp.float32)

    cotan_all = lax.all_gather(cotan, "dp", axis=1, tiled=True)
    part = jnp.einsum(
        "mjik,dk->jmid",
        cotan_all.reshape(mb, n_dp * n_t, tok_dev, width_t),
        weight,
        preferred_element_type=jnp.float32,
    ).astype(jnp.bfloat16)
    got = lax.all_to_all(part, ("dp", "tensor"), 0, 0, tiled=True)
    got = got.reshape(n_dp, n_t, mb, tok_dev, rows_p).astype(jnp.float32)
    normed_grad = got[:, 0]
    for t in range(1, n_t):
        normed_grad = normed_grad + got[:, t]
    normed_grad = normed_grad.transpose(1, 2, 0, 3).reshape(mb, tok_dev, d_model)

    hidden_gradient = normed_grad * gain_float
    branch_path = inverse_scale * (
        hidden_gradient
        - centered_input * jnp.mean(hidden_gradient * centered_input, axis=-1, keepdims=True)
    )
    later = later_sum(branch_path)
    grad_in = (top_grad.astype(jnp.float32) + branch_path + later).astype(jnp.bfloat16)

    own_input, own_gain = lax.optimization_barrier((saved_input[0], norm_gain[0]))
    own_float = own_input.astype(jnp.float32)
    own_scale = lax.rsqrt(jnp.mean(own_float * own_float, axis=-1, keepdims=True) + 1e-05)
    own_normed = ((own_float * own_scale) * own_gain.astype(jnp.float32)).astype(jnp.bfloat16)
    nrm_blocks = own_normed.reshape(mb, tok_dev, n_dp, rows_p)
    pieces = [lax.dynamic_index_in_dim(nrm_blocks, my_p, 2, False)]
    for k in range(1, n_dp):
        send = lax.dynamic_index_in_dim(nrm_blocks, (my_p + k) % n_dp, 2, False)
        pieces.append(
            lax.ppermute(send, "dp", [(q, (q + k) % n_dp) for q in range(n_dp)])
        )
    nrm = lax.all_gather(jnp.stack(pieces), "tensor", axis=0, tiled=False)
    cot = cotan_all.reshape(mb, n_dp, n_t, tok_dev, width_t)
    cot_rev = jnp.concatenate([cot[:, ::-1], cot[:, ::-1]], axis=1)
    cot_sel = lax.dynamic_slice_in_dim(cot_rev, n_dp - 1 - my_p, n_dp, axis=1)
    groups = (my_p - jnp.arange(n_dp, dtype=jnp.int32)) % n_dp

    row_ids = my_p * jnp.int32(rows_p) + jnp.arange(rows_p, dtype=jnp.int32)
    index = (
        row_ids[:, None] * jnp.int32(total_cols)
        + my_t * jnp.int32(width_t)
        + jnp.arange(width_t, dtype=jnp.int32)[None, :]
    )
    terms = jnp.einsum("tkmid,mktic->kdc", nrm, cot_sel, preferred_element_type=jnp.float32)
    rounded = dither(terms, salt, counter, layer, groups[:, None, None], index[None])
    wsum = jnp.sum(rounded, axis=0)
    return (grad_in[None], wsum[None])


def solution(mesh):
    placed = (
        P("section", None, ("dp", "tensor"), None),
        P("section", None, "dp", "tensor"),
        P("section", "dp", "tensor"),
        P("section", None),
        P(None, ("dp", "tensor"), None),
        P(),
        P(),
    )
    return jax.shard_map(
        body,
        mesh=mesh,
        in_specs=placed,
        out_specs=(P("section", None, ("dp", "tensor"), None), P("section", "dp", "tensor")),
        check_vma=False,
    )
```

```python
import jax
import jax.numpy as jnp
from jax import lax
from jax.sharding import PartitionSpec as P


def mix_bits(salt, counter, layer, group, index):
    h = (
        index * jnp.int32(-1640531535)
        + salt * jnp.int32(374761393)
        + counter * jnp.int32(668265263)
    )
    h = h + layer * jnp.int32(-1028477379) + group * jnp.int32(1274126177)
    h = h ^ lax.shift_right_logical(h, jnp.int32(16))
    h = h * jnp.int32(2146121005)
    h = h ^ lax.shift_right_logical(h, jnp.int32(15))
    h = h * jnp.int32(-2073254261)
    h = h ^ lax.shift_right_logical(h, jnp.int32(16))
    return lax.shift_right_logical(h, jnp.int32(8)).astype(jnp.float32) * (1.0 / 16777216.0)


def dither(term, salt, counter, layer, group, index):
    noise = mix_bits(salt, counter, layer, group, index)
    moved = term * (1.0 + (noise - 0.5) * 0.5)
    return lax.optimization_barrier(moved.astype(jnp.bfloat16)).astype(jnp.float32)


def later_sum(branch_path):
    n_sec = lax.axis_size("section")
    m, t, d = branch_path.shape
    rt = t // 8
    half = n_sec // (m * rt)
    w = d // half
    chunks = branch_path.astype(jnp.bfloat16).reshape(m, rt, 8, half, w)
    chunks = chunks.transpose(0, 1, 3, 2, 4).reshape(n_sec, 8, w)
    got = lax.all_to_all(chunks, "section", 0, 0, tiled=True)
    src = jnp.arange(n_sec, dtype=jnp.int32)
    upper = (src[None, :] > src[:, None]).astype(jnp.bfloat16)
    suffix = jnp.einsum(
        "st,tx->sx", upper, got.reshape(n_sec, -1), preferred_element_type=jnp.float32
    )
    back = lax.all_to_all(
        suffix.astype(jnp.bfloat16).reshape(n_sec, 8, w), "section", 0, 0, tiled=True
    )
    back = back.reshape(m, rt, half, 8, w).transpose(0, 1, 3, 2, 4)
    return back.reshape(m, t, d).astype(jnp.float32)


def body(saved_input, kv_grad, kv_weight, norm_gain, top_grad, noise_salt, step_counter):
    salt = noise_salt[0]
    counter = step_counter[0]
    layer = lax.axis_index("section")
    n_dp = lax.axis_size("dp")
    n_t = lax.axis_size("tensor")
    my_p = lax.axis_index("dp")
    my_t = lax.axis_index("tensor")
    cotan = kv_grad[0]
    weight = kv_weight[0]
    rows_p, width_t = weight.shape
    total_cols = width_t * n_t
    mb, tok_dev, d_model = saved_input.shape[1:]

    input_float = saved_input[0].astype(jnp.float32)
    inverse_scale = lax.rsqrt(jnp.mean(input_float * input_float, axis=-1, keepdims=True) + 1e-05)
    centered_input = input_float * inverse_scale
    gain_float = norm_gain[0].astype(jnp.float32)

    cotan_all = lax.all_gather(cotan, "dp", axis=1, tiled=True)
    part = jnp.einsum(
        "mjik,dk->jmid",
        cotan_all.reshape(mb, n_dp * n_t, tok_dev, width_t),
        weight,
        preferred_element_type=jnp.float32,
    ).astype(jnp.bfloat16)
    part = part.reshape(n_dp, n_t // 2, 2, mb, tok_dev, rows_p)
    my_core = my_t % 2
    my_hi = my_t // 2
    keep = lax.dynamic_index_in_dim(part, my_core, 2, False)
    send = lax.dynamic_index_in_dim(part, 1 - my_core, 2, False)
    recv = lax.ppermute(send, "tensor", [(q, q ^ 1) for q in range(n_t)])
    pair = keep.astype(jnp.float32) + recv.astype(jnp.float32)
    keep = lax.dynamic_index_in_dim(pair, my_hi, 1, False)
    send = lax.dynamic_index_in_dim(pair, 1 - my_hi, 1, False)
    recv = lax.ppermute(send, "tensor", [(q, q ^ 2) for q in range(n_t)])
    total = (keep + recv).astype(jnp.bfloat16)
    got = lax.all_to_all(total, "dp", 0, 0, tiled=True)
    normed_grad = got.astype(jnp.float32).transpose(1, 2, 0, 3).reshape(mb, tok_dev, d_model)

    hidden_gradient = normed_grad * gain_float
    branch_path = inverse_scale * (
        hidden_gradient
        - centered_input * jnp.mean(hidden_gradient * centered_input, axis=-1, keepdims=True)
    )
    later = later_sum(branch_path)
    grad_in = (top_grad.astype(jnp.float32) + branch_path + later).astype(jnp.bfloat16)

    own_input, own_gain = lax.optimization_barrier((saved_input[0], norm_gain[0]))
    own_float = own_input.astype(jnp.float32)
    own_scale = lax.rsqrt(jnp.mean(own_float * own_float, axis=-1, keepdims=True) + 1e-05)
    own_normed = ((own_float * own_scale) * own_gain.astype(jnp.float32)).astype(jnp.bfloat16)
    nrm_blocks = own_normed.reshape(mb, tok_dev, n_dp, rows_p)
    pieces = [lax.dynamic_index_in_dim(nrm_blocks, my_p, 2, False)]
    for k in range(1, n_dp):
        send = lax.dynamic_index_in_dim(nrm_blocks, (my_p + k) % n_dp, 2, False)
        pieces.append(
            lax.ppermute(send, "dp", [(q, (q + k) % n_dp) for q in range(n_dp)])
        )
    nrm = lax.all_gather(jnp.stack(pieces), "tensor", axis=0, tiled=False)
    cot = cotan_all.reshape(mb, n_dp, n_t, tok_dev, width_t)
    cot_rev = jnp.concatenate([cot[:, ::-1], cot[:, ::-1]], axis=1)
    cot_sel = lax.dynamic_slice_in_dim(cot_rev, n_dp - 1 - my_p, n_dp, axis=1)
    groups = (my_p - jnp.arange(n_dp, dtype=jnp.int32)) % n_dp

    row_ids = my_p * jnp.int32(rows_p) + jnp.arange(rows_p, dtype=jnp.int32)
    index = (
        row_ids[:, None] * jnp.int32(total_cols)
        + my_t * jnp.int32(width_t)
        + jnp.arange(width_t, dtype=jnp.int32)[None, :]
    )
    terms = jnp.einsum("tkmid,mktic->kdc", nrm, cot_sel, preferred_element_type=jnp.float32)
    rounded = dither(terms, salt, counter, layer, groups[:, None, None], index[None])
    wsum = jnp.sum(rounded, axis=0)
    return (grad_in[None], wsum[None])


def solution(mesh):
    placed = (
        P("section", None, ("dp", "tensor"), None),
        P("section", None, "dp", "tensor"),
        P("section", "dp", "tensor"),
        P("section", None),
        P(None, ("dp", "tensor"), None),
        P(),
        P(),
    )
    return jax.shard_map(
        body,
        mesh=mesh,
        in_specs=placed,
        out_specs=(P("section", None, ("dp", "tensor"), None), P("section", "dp", "tensor")),
        check_vma=False,
    )
```

```python
import jax
import jax.numpy as jnp
from jax import lax
from jax.sharding import PartitionSpec as P


def mix_bits(salt, counter, layer, group, index):
    h = (
        index * jnp.int32(-1640531535)
        + salt * jnp.int32(374761393)
        + counter * jnp.int32(668265263)
    )
    h = h + layer * jnp.int32(-1028477379) + group * jnp.int32(1274126177)
    h = h ^ lax.shift_right_logical(h, jnp.int32(16))
    h = h * jnp.int32(2146121005)
    h = h ^ lax.shift_right_logical(h, jnp.int32(15))
    h = h * jnp.int32(-2073254261)
    h = h ^ lax.shift_right_logical(h, jnp.int32(16))
    return lax.shift_right_logical(h, jnp.int32(8)).astype(jnp.float32) * (1.0 / 16777216.0)


def dither(term, salt, counter, layer, group, index):
    noise = mix_bits(salt, counter, layer, group, index)
    moved = term * (1.0 + (noise - 0.5) * 0.5)
    return lax.optimization_barrier(moved.astype(jnp.bfloat16)).astype(jnp.float32)


def later_sum(branch_path):
    n_sec = lax.axis_size("section")
    m, t, d = branch_path.shape
    rt = t // 8
    half = n_sec // (m * rt)
    w = d // half
    chunks = branch_path.astype(jnp.bfloat16).reshape(m, rt, 8, half, w)
    chunks = chunks.transpose(0, 1, 3, 2, 4).reshape(n_sec, 8, w)
    got = lax.all_to_all(chunks, "section", 0, 0, tiled=True)
    src = jnp.arange(n_sec, dtype=jnp.int32)
    upper = (src[None, :] > src[:, None]).astype(jnp.bfloat16)
    suffix = jnp.einsum(
        "st,tx->sx", upper, got.reshape(n_sec, -1), preferred_element_type=jnp.float32
    )
    back = lax.all_to_all(
        suffix.astype(jnp.bfloat16).reshape(n_sec, 8, w), "section", 0, 0, tiled=True
    )
    back = back.reshape(m, rt, half, 8, w).transpose(0, 1, 3, 2, 4)
    return back.reshape(m, t, d).astype(jnp.float32)


def body(saved_input, kv_grad, kv_weight, norm_gain, top_grad, noise_salt, step_counter):
    salt = noise_salt[0]
    counter = step_counter[0]
    layer = lax.axis_index("section")
    n_dp = lax.axis_size("dp")
    n_t = lax.axis_size("tensor")
    my_p = lax.axis_index("dp")
    my_t = lax.axis_index("tensor")
    my_core = my_t % 2
    my_hi = my_t // 2
    cotan = kv_grad[0]
    weight = kv_weight[0]
    rows_p, width_t = weight.shape
    total_cols = width_t * n_t
    mb, tok_dev, d_model = saved_input.shape[1:]

    input_float = saved_input[0].astype(jnp.float32)
    inverse_scale = lax.rsqrt(jnp.mean(input_float * input_float, axis=-1, keepdims=True) + 1e-05)
    centered_input = input_float * inverse_scale
    gain_float = norm_gain[0].astype(jnp.float32)

    kv_pieces = [cotan]
    for k in range(1, n_dp):
        kv_pieces.append(
            lax.ppermute(cotan, "dp", [(q, (q + k) % n_dp) for q in range(n_dp)])
        )
    kv_sel = jnp.stack(kv_pieces)
    kv_rev = jnp.concatenate([kv_sel[::-1], kv_sel[::-1]], axis=0)
    cotan_all = lax.dynamic_slice_in_dim(kv_rev, n_dp - 1 - my_p, n_dp, axis=0)
    cotan_all = cotan_all.transpose(1, 0, 2, 3).reshape(mb, n_dp * cotan.shape[1], width_t)
    part = jnp.einsum(
        "mjik,dk->jmid",
        cotan_all.reshape(mb, n_dp * n_t, tok_dev, width_t),
        weight,
        preferred_element_type=jnp.float32,
    ).astype(jnp.bfloat16)
    part = part.reshape(n_dp, n_t // 2, 2, mb, tok_dev, rows_p)
    keep = lax.dynamic_index_in_dim(part, my_core, 2, False)
    send = lax.dynamic_index_in_dim(part, 1 - my_core, 2, False)
    recv = lax.ppermute(send, "tensor", [(q, q ^ 1) for q in range(n_t)])
    pair = (keep.astype(jnp.float32) + recv.astype(jnp.float32)).astype(jnp.bfloat16)
    keep = lax.dynamic_index_in_dim(pair, my_hi, 1, False)
    send = lax.dynamic_index_in_dim(pair, 1 - my_hi, 1, False)
    recv = lax.ppermute(send, "tensor", [(q, q ^ 2) for q in range(n_t)])
    total = (keep.astype(jnp.float32) + recv.astype(jnp.float32)).astype(jnp.bfloat16)
    got = lax.all_to_all(total, "dp", 0, 0, tiled=True)
    normed_grad = got.astype(jnp.float32).transpose(1, 2, 0, 3).reshape(mb, tok_dev, d_model)

    hidden_gradient = normed_grad * gain_float
    branch_path = inverse_scale * (
        hidden_gradient
        - centered_input * jnp.mean(hidden_gradient * centered_input, axis=-1, keepdims=True)
    )
    later = later_sum(branch_path)
    grad_in = (top_grad.astype(jnp.float32) + branch_path + later).astype(jnp.bfloat16)

    own_input, own_gain = lax.optimization_barrier((saved_input[0], norm_gain[0]))
    own_float = own_input.astype(jnp.float32)
    own_scale = lax.rsqrt(jnp.mean(own_float * own_float, axis=-1, keepdims=True) + 1e-05)
    own_normed = ((own_float * own_scale) * own_gain.astype(jnp.float32)).astype(jnp.bfloat16)
    nrm_blocks = own_normed.reshape(mb, tok_dev, n_dp, rows_p)
    pieces = [lax.dynamic_index_in_dim(nrm_blocks, my_p, 2, False)]
    for k in range(1, n_dp):
        send = lax.dynamic_index_in_dim(nrm_blocks, (my_p + k) % n_dp, 2, False)
        pieces.append(
            lax.ppermute(send, "dp", [(q, (q + k) % n_dp) for q in range(n_dp)])
        )
    mine = jnp.stack(pieces)
    far = lax.ppermute(mine, "tensor", [(q, q ^ 2) for q in range(n_t)])
    on_chip = jnp.stack([mine, far])
    hi_order = jnp.where(my_hi == 0, on_chip, on_chip[::-1])
    other = lax.ppermute(hi_order, "tensor", [(q, q ^ 1) for q in range(n_t)])
    both = jnp.where(my_core == 0, jnp.stack([hi_order, other]), jnp.stack([other, hi_order]))
    nrm = both.transpose(1, 0, 2, 3, 4, 5).reshape((n_t,) + mine.shape)
    cot_sel = kv_sel.reshape(n_dp, mb, n_t, tok_dev, width_t).transpose(1, 0, 2, 3, 4)
    groups = (my_p - jnp.arange(n_dp, dtype=jnp.int32)) % n_dp

    row_ids = my_p * jnp.int32(rows_p) + jnp.arange(rows_p, dtype=jnp.int32)
    index = (
        row_ids[:, None] * jnp.int32(total_cols)
        + my_t * jnp.int32(width_t)
        + jnp.arange(width_t, dtype=jnp.int32)[None, :]
    )
    terms = jnp.einsum("tkmid,mktic->kdc", nrm, cot_sel, preferred_element_type=jnp.float32)
    rounded = dither(terms, salt, counter, layer, groups[:, None, None], index[None])
    wsum = jnp.sum(rounded, axis=0)
    return (grad_in[None], wsum[None])


def solution(mesh):
    placed = (
        P("section", None, ("dp", "tensor"), None),
        P("section", None, "dp", "tensor"),
        P("section", "dp", "tensor"),
        P("section", None),
        P(None, ("dp", "tensor"), None),
        P(),
        P(),
    )
    return jax.shard_map(
        body,
        mesh=mesh,
        in_specs=placed,
        out_specs=(P("section", None, ("dp", "tensor"), None), P("section", "dp", "tensor")),
        check_vma=False,
    )
```

```python
import jax
import jax.numpy as jnp
from jax import lax
from jax.sharding import PartitionSpec as P


def mix_bits(salt, counter, layer, group, index):
    h = (
        index * jnp.int32(-1640531535)
        + salt * jnp.int32(374761393)
        + counter * jnp.int32(668265263)
    )
    h = h + layer * jnp.int32(-1028477379) + group * jnp.int32(1274126177)
    h = h ^ lax.shift_right_logical(h, jnp.int32(16))
    h = h * jnp.int32(2146121005)
    h = h ^ lax.shift_right_logical(h, jnp.int32(15))
    h = h * jnp.int32(-2073254261)
    h = h ^ lax.shift_right_logical(h, jnp.int32(16))
    return lax.shift_right_logical(h, jnp.int32(8)).astype(jnp.float32) * (1.0 / 16777216.0)


def dither(term, salt, counter, layer, group, index):
    noise = mix_bits(salt, counter, layer, group, index)
    moved = term * (1.0 + (noise - 0.5) * 0.5)
    return lax.optimization_barrier(moved.astype(jnp.bfloat16)).astype(jnp.float32)


def roll_in(stacked, shift, n):
    rev = jnp.concatenate([stacked[::-1], stacked[::-1]], axis=0)
    return lax.dynamic_slice_in_dim(rev, (n - 1 - shift) % n, n, axis=0)


def later_sum(branch_path):
    n_sec = lax.axis_size("section")
    n_z = n_sec // 2
    my_s = lax.axis_index("section")
    my_z = my_s // 2
    my_lo = my_s % 2
    _, t, d = branch_path.shape
    bb = branch_path.astype(jnp.bfloat16)
    partner = lax.ppermute(bb, "section", [(q, q ^ 1) for q in range(n_sec)])
    pair = (bb.astype(jnp.float32) + partner.astype(jnp.float32)).astype(jnp.bfloat16)
    half = lax.dynamic_index_in_dim(pair, my_lo, 0, False).reshape(t, n_z, d // n_z)
    half = half.transpose(1, 0, 2)
    got = [lax.dynamic_index_in_dim(half, my_z, 0, False)]
    for k in range(1, n_z):
        send = lax.dynamic_index_in_dim(half, (my_z + k) % n_z, 0, False)
        got.append(lax.ppermute(send, "section", [(q, (q + 2 * k) % n_sec) for q in range(n_sec)]))
    by_src = roll_in(jnp.stack(got), my_z, n_z)
    src = jnp.arange(n_z, dtype=jnp.int32)
    upper = (src[None, :] > src[:, None]).astype(jnp.bfloat16)
    suffix = jnp.einsum(
        "st,tx->sx", upper, by_src.reshape(n_z, -1), preferred_element_type=jnp.float32
    ).astype(jnp.bfloat16).reshape(by_src.shape)
    back = [lax.dynamic_index_in_dim(suffix, my_z, 0, False)]
    for k in range(1, n_z):
        send = lax.dynamic_index_in_dim(suffix, (my_z + k) % n_z, 0, False)
        back.append(lax.ppermute(send, "section", [(q, (q + 2 * k) % n_sec) for q in range(n_sec)]))
    mine = roll_in(jnp.stack(back), my_z, n_z).transpose(1, 0, 2).reshape(t, d)
    theirs = lax.ppermute(mine, "section", [(q, q ^ 1) for q in range(n_sec)])
    both = jnp.where(my_lo == 0, jnp.stack([mine, theirs]), jnp.stack([theirs, mine]))
    extra = jnp.where(my_lo == 0, partner.astype(jnp.float32), 0.0)
    return both.astype(jnp.float32) + extra


def body(saved_input, kv_grad, kv_weight, norm_gain, top_grad, noise_salt, step_counter):
    salt = noise_salt[0]
    counter = step_counter[0]
    layer = lax.axis_index("section")
    n_dp = lax.axis_size("dp")
    n_t = lax.axis_size("tensor")
    my_p = lax.axis_index("dp")
    my_t = lax.axis_index("tensor")
    my_core = my_t % 2
    my_hi = my_t // 2
    cotan = kv_grad[0]
    weight = kv_weight[0]
    rows_p, width_t = weight.shape
    total_cols = width_t * n_t
    mb, tok_dev, d_model = saved_input.shape[1:]

    input_float = saved_input[0].astype(jnp.float32)
    inverse_scale = lax.rsqrt(jnp.mean(input_float * input_float, axis=-1, keepdims=True) + 1e-05)
    centered_input = input_float * inverse_scale
    gain_float = norm_gain[0].astype(jnp.float32)

    kv_pieces = [cotan]
    for k in range(1, n_dp):
        kv_pieces.append(
            lax.ppermute(cotan, "dp", [(q, (q + k) % n_dp) for q in range(n_dp)])
        )
    kv_sel = jnp.stack(kv_pieces)
    kv_rev = jnp.concatenate([kv_sel[::-1], kv_sel[::-1]], axis=0)
    cotan_all = lax.dynamic_slice_in_dim(kv_rev, n_dp - 1 - my_p, n_dp, axis=0)
    cotan_all = cotan_all.transpose(1, 0, 2, 3).reshape(mb, n_dp * cotan.shape[1], width_t)
    part = jnp.einsum(
        "mjik,dk->jmid",
        cotan_all.reshape(mb, n_dp * n_t, tok_dev, width_t),
        weight,
        preferred_element_type=jnp.float32,
    ).astype(jnp.bfloat16)
    part = part.reshape(n_dp, n_t // 2, 2, mb, tok_dev, rows_p)
    keep = lax.dynamic_index_in_dim(part, my_core, 2, False)
    send = lax.dynamic_index_in_dim(part, 1 - my_core, 2, False)
    recv = lax.ppermute(send, "tensor", [(q, q ^ 1) for q in range(n_t)])
    pair = (keep.astype(jnp.float32) + recv.astype(jnp.float32)).astype(jnp.bfloat16)
    keep = lax.dynamic_index_in_dim(pair, my_hi, 1, False)
    send = lax.dynamic_index_in_dim(pair, 1 - my_hi, 1, False)
    recv = lax.ppermute(send, "tensor", [(q, q ^ 2) for q in range(n_t)])
    total = (keep.astype(jnp.float32) + recv.astype(jnp.float32)).astype(jnp.bfloat16)
    got = lax.all_to_all(total, "dp", 0, 0, tiled=True)
    normed_grad = got.astype(jnp.float32).transpose(1, 2, 0, 3).reshape(mb, tok_dev, d_model)

    hidden_gradient = normed_grad * gain_float
    branch_path = inverse_scale * (
        hidden_gradient
        - centered_input * jnp.mean(hidden_gradient * centered_input, axis=-1, keepdims=True)
    )
    later = later_sum(branch_path)
    grad_in = (top_grad.astype(jnp.float32) + branch_path + later).astype(jnp.bfloat16)

    own_input, own_gain = lax.optimization_barrier((saved_input[0], norm_gain[0]))
    own_float = own_input.astype(jnp.float32)
    own_scale = lax.rsqrt(jnp.mean(own_float * own_float, axis=-1, keepdims=True) + 1e-05)
    own_normed = ((own_float * own_scale) * own_gain.astype(jnp.float32)).astype(jnp.bfloat16)
    nrm_blocks = own_normed.reshape(mb, tok_dev, n_dp, rows_p)
    pieces = [lax.dynamic_index_in_dim(nrm_blocks, my_p, 2, False)]
    for k in range(1, n_dp):
        send = lax.dynamic_index_in_dim(nrm_blocks, (my_p + k) % n_dp, 2, False)
        pieces.append(
            lax.ppermute(send, "dp", [(q, (q + k) % n_dp) for q in range(n_dp)])
        )
    mine = jnp.stack(pieces)
    far = lax.ppermute(mine, "tensor", [(q, q ^ 2) for q in range(n_t)])
    on_chip = jnp.stack([mine, far])
    hi_order = jnp.where(my_hi == 0, on_chip, on_chip[::-1])
    other = lax.ppermute(hi_order, "tensor", [(q, q ^ 1) for q in range(n_t)])
    both = jnp.where(my_core == 0, jnp.stack([hi_order, other]), jnp.stack([other, hi_order]))
    nrm = both.transpose(1, 0, 2, 3, 4, 5).reshape((n_t,) + mine.shape)
    cot_sel = kv_sel.reshape(n_dp, mb, n_t, tok_dev, width_t).transpose(1, 0, 2, 3, 4)
    groups = (my_p - jnp.arange(n_dp, dtype=jnp.int32)) % n_dp

    row_ids = my_p * jnp.int32(rows_p) + jnp.arange(rows_p, dtype=jnp.int32)
    index = (
        row_ids[:, None] * jnp.int32(total_cols)
        + my_t * jnp.int32(width_t)
        + jnp.arange(width_t, dtype=jnp.int32)[None, :]
    )
    terms = jnp.einsum("tkmid,mktic->kdc", nrm, cot_sel, preferred_element_type=jnp.float32)
    rounded = dither(terms, salt, counter, layer, groups[:, None, None], index[None])
    wsum = jnp.sum(rounded, axis=0)
    return (grad_in[None], wsum[None])


def solution(mesh):
    placed = (
        P("section", None, ("dp", "tensor"), None),
        P("section", None, "dp", "tensor"),
        P("section", "dp", "tensor"),
        P("section", None),
        P(None, ("dp", "tensor"), None),
        P(),
        P(),
    )
    return jax.shard_map(
        body,
        mesh=mesh,
        in_specs=placed,
        out_specs=(P("section", None, ("dp", "tensor"), None), P("section", "dp", "tensor")),
        check_vma=False,
    )
```

```python
import jax
import jax.numpy as jnp
from jax import lax
from jax.sharding import PartitionSpec as P


def mix_bits(salt, counter, layer, group, index):
    h = (
        index * jnp.int32(-1640531535)
        + salt * jnp.int32(374761393)
        + counter * jnp.int32(668265263)
    )
    h = h + layer * jnp.int32(-1028477379) + group * jnp.int32(1274126177)
    h = h ^ lax.shift_right_logical(h, jnp.int32(16))
    h = h * jnp.int32(2146121005)
    h = h ^ lax.shift_right_logical(h, jnp.int32(15))
    h = h * jnp.int32(-2073254261)
    h = h ^ lax.shift_right_logical(h, jnp.int32(16))
    return lax.shift_right_logical(h, jnp.int32(8)).astype(jnp.float32) * (1.0 / 16777216.0)


def dither(term, salt, counter, layer, group, index):
    noise = mix_bits(salt, counter, layer, group, index)
    moved = term * (1.0 + (noise - 0.5) * 0.5)
    return lax.optimization_barrier(moved.astype(jnp.bfloat16)).astype(jnp.float32)


def later_sum(branch_path):
    n_sec = lax.axis_size("section")
    m, t, d = branch_path.shape
    rt = t // 8
    half = n_sec // (m * rt)
    w = d // half
    chunks = branch_path.astype(jnp.bfloat16).reshape(m, rt, 8, half, w)
    chunks = chunks.transpose(0, 1, 3, 2, 4).reshape(n_sec, 8, w)
    got = lax.all_to_all(chunks, "section", 0, 0, tiled=True)
    shifted = jnp.concatenate([got[1:], jnp.zeros_like(got[:1])], axis=0)
    suffix = lax.cumsum(shifted.astype(jnp.float32), axis=0, reverse=True)
    back = lax.all_to_all(suffix.astype(jnp.bfloat16), "section", 0, 0, tiled=True)
    back = back.reshape(m, rt, half, 8, w).transpose(0, 1, 3, 2, 4)
    return back.reshape(m, t, d).astype(jnp.float32)


def body(saved_input, kv_grad, kv_weight, norm_gain, top_grad, noise_salt, step_counter):
    salt = noise_salt[0]
    counter = step_counter[0]
    layer = lax.axis_index("section")
    n_dp = lax.axis_size("dp")
    n_t = lax.axis_size("tensor")
    my_p = lax.axis_index("dp")
    my_t = lax.axis_index("tensor")
    my_core = my_t % 2
    my_hi = my_t // 2
    cotan = kv_grad[0]
    weight = kv_weight[0]
    rows_p, width_t = weight.shape
    total_cols = width_t * n_t
    mb, tok_dev, d_model = saved_input.shape[1:]

    input_float = saved_input[0].astype(jnp.float32)
    inverse_scale = lax.rsqrt(jnp.mean(input_float * input_float, axis=-1, keepdims=True) + 1e-05)
    centered_input = input_float * inverse_scale
    gain_float = norm_gain[0].astype(jnp.float32)

    kv_pieces = [cotan]
    for k in range(1, n_dp):
        kv_pieces.append(
            lax.ppermute(cotan, "dp", [(q, (q + k) % n_dp) for q in range(n_dp)])
        )
    kv_sel = jnp.stack(kv_pieces)
    kv_rev = jnp.concatenate([kv_sel[::-1], kv_sel[::-1]], axis=0)
    cotan_all = lax.dynamic_slice_in_dim(kv_rev, n_dp - 1 - my_p, n_dp, axis=0)
    cotan_all = cotan_all.transpose(1, 0, 2, 3).reshape(mb, n_dp * cotan.shape[1], width_t)
    part = jnp.einsum(
        "mjik,dk->jmid",
        cotan_all.reshape(mb, n_dp * n_t, tok_dev, width_t),
        weight,
        preferred_element_type=jnp.float32,
    ).astype(jnp.bfloat16)
    part = part.reshape(n_dp, n_t // 2, 2, mb, tok_dev, rows_p)
    keep = lax.dynamic_index_in_dim(part, my_core, 2, False)
    send = lax.dynamic_index_in_dim(part, 1 - my_core, 2, False)
    recv = lax.ppermute(send, "tensor", [(q, q ^ 1) for q in range(n_t)])
    pair = (keep.astype(jnp.float32) + recv.astype(jnp.float32)).astype(jnp.bfloat16)
    keep = lax.dynamic_index_in_dim(pair, my_hi, 1, False)
    send = lax.dynamic_index_in_dim(pair, 1 - my_hi, 1, False)
    recv = lax.ppermute(send, "tensor", [(q, q ^ 2) for q in range(n_t)])
    total = (keep.astype(jnp.float32) + recv.astype(jnp.float32)).astype(jnp.bfloat16)
    got = lax.all_to_all(total, "dp", 0, 0, tiled=True)
    normed_grad = got.astype(jnp.float32).transpose(1, 2, 0, 3).reshape(mb, tok_dev, d_model)

    hidden_gradient = normed_grad * gain_float
    branch_path = inverse_scale * (
        hidden_gradient
        - centered_input * jnp.mean(hidden_gradient * centered_input, axis=-1, keepdims=True)
    )
    later = later_sum(branch_path)
    grad_in = (top_grad.astype(jnp.float32) + branch_path + later).astype(jnp.bfloat16)

    own_input, own_gain = lax.optimization_barrier((saved_input[0], norm_gain[0]))
    own_float = own_input.astype(jnp.float32)
    own_scale = lax.rsqrt(jnp.mean(own_float * own_float, axis=-1, keepdims=True) + 1e-05)
    own_normed = ((own_float * own_scale) * own_gain.astype(jnp.float32)).astype(jnp.bfloat16)
    nrm_blocks = own_normed.reshape(mb, tok_dev, n_dp, rows_p)
    pieces = [lax.dynamic_index_in_dim(nrm_blocks, my_p, 2, False)]
    for k in range(1, n_dp):
        send = lax.dynamic_index_in_dim(nrm_blocks, (my_p + k) % n_dp, 2, False)
        pieces.append(
            lax.ppermute(send, "dp", [(q, (q + k) % n_dp) for q in range(n_dp)])
        )
    mine = jnp.stack(pieces)
    far = lax.ppermute(mine, "tensor", [(q, q ^ 2) for q in range(n_t)])
    on_chip = jnp.stack([mine, far])
    hi_order = jnp.where(my_hi == 0, on_chip, on_chip[::-1])
    other = lax.ppermute(hi_order, "tensor", [(q, q ^ 1) for q in range(n_t)])
    both = jnp.where(my_core == 0, jnp.stack([hi_order, other]), jnp.stack([other, hi_order]))
    nrm = both.transpose(1, 0, 2, 3, 4, 5).reshape((n_t,) + mine.shape)
    cot_sel = kv_sel.reshape(n_dp, mb, n_t, tok_dev, width_t).transpose(1, 0, 2, 3, 4)
    groups = (my_p - jnp.arange(n_dp, dtype=jnp.int32)) % n_dp

    row_ids = my_p * jnp.int32(rows_p) + jnp.arange(rows_p, dtype=jnp.int32)
    index = (
        row_ids[:, None] * jnp.int32(total_cols)
        + my_t * jnp.int32(width_t)
        + jnp.arange(width_t, dtype=jnp.int32)[None, :]
    )
    terms = jnp.einsum("tkmid,mktic->kdc", nrm, cot_sel, preferred_element_type=jnp.float32)
    rounded = dither(terms, salt, counter, layer, groups[:, None, None], index[None])
    wsum = jnp.sum(rounded, axis=0)
    return (grad_in[None], wsum[None])


def solution(mesh):
    placed = (
        P("section", None, ("dp", "tensor"), None),
        P("section", None, "dp", "tensor"),
        P("section", "dp", "tensor"),
        P("section", None),
        P(None, ("dp", "tensor"), None),
        P(),
        P(),
    )
    return jax.shard_map(
        body,
        mesh=mesh,
        in_specs=placed,
        out_specs=(P("section", None, ("dp", "tensor"), None), P("section", "dp", "tensor")),
        check_vma=False,
    )
```

```python
import jax
import jax.numpy as jnp
from jax import lax
from jax.sharding import PartitionSpec as P


def mix_bits(salt, counter, layer, group, index):
    h = (
        index * jnp.int32(-1640531535)
        + salt * jnp.int32(374761393)
        + counter * jnp.int32(668265263)
    )
    h = h + layer * jnp.int32(-1028477379) + group * jnp.int32(1274126177)
    h = h ^ lax.shift_right_logical(h, jnp.int32(16))
    h = h * jnp.int32(2146121005)
    h = h ^ lax.shift_right_logical(h, jnp.int32(15))
    h = h * jnp.int32(-2073254261)
    h = h ^ lax.shift_right_logical(h, jnp.int32(16))
    return lax.shift_right_logical(h, jnp.int32(8)).astype(jnp.float32) * (1.0 / 16777216.0)


def dither(term, salt, counter, layer, group, index):
    noise = mix_bits(salt, counter, layer, group, index)
    moved = term * (1.0 + (noise - 0.5) * 0.5)
    return lax.optimization_barrier(moved.astype(jnp.bfloat16)).astype(jnp.float32)


def later_sum(branch4):
    n_sec = lax.axis_size("section")
    chunks = branch4.astype(jnp.bfloat16).reshape(n_sec, -1, branch4.shape[-1])
    got = lax.all_to_all(chunks, "section", 0, 0, tiled=True)
    shifted = jnp.concatenate([got[1:], jnp.zeros_like(got[:1])], axis=0)
    suffix = lax.cumsum(shifted.astype(jnp.float32), axis=0, reverse=True)
    back = lax.all_to_all(suffix.astype(jnp.bfloat16), "section", 0, 0, tiled=True)
    return back.reshape(branch4.shape).astype(jnp.float32)


def body(saved_input, kv_grad, kv_weight, norm_gain, top_grad, noise_salt, step_counter):
    salt = noise_salt[0]
    counter = step_counter[0]
    layer = lax.axis_index("section")
    n_dp = lax.axis_size("dp")
    n_t = lax.axis_size("tensor")
    my_p = lax.axis_index("dp")
    my_t = lax.axis_index("tensor")
    my_core = my_t % 2
    my_hi = my_t // 2
    cotan = kv_grad[0]
    weight = kv_weight[0]
    rows_p, width_t = weight.shape
    total_cols = width_t * n_t
    mb, tok_dev, d_model = saved_input.shape[1:]

    input_float = saved_input[0].astype(jnp.float32)
    inverse_scale = lax.rsqrt(jnp.mean(input_float * input_float, axis=-1, keepdims=True) + 1e-05)
    gain_float = norm_gain[0].astype(jnp.float32)

    kv_pieces = [cotan]
    for k in range(1, n_dp):
        kv_pieces.append(
            lax.ppermute(cotan, "dp", [(q, (q + k) % n_dp) for q in range(n_dp)])
        )
    kv_sel = jnp.stack(kv_pieces)
    kv_rev = jnp.concatenate([kv_sel[::-1], kv_sel[::-1]], axis=0)
    cotan_all = lax.dynamic_slice_in_dim(kv_rev, n_dp - 1 - my_p, n_dp, axis=0)
    cotan_all = cotan_all.transpose(1, 0, 2, 3).reshape(mb, n_dp * cotan.shape[1], width_t)
    part = jnp.einsum(
        "mjik,dk->jmid",
        cotan_all.reshape(mb, n_dp * n_t, tok_dev, width_t),
        weight,
        preferred_element_type=jnp.float32,
    ).astype(jnp.bfloat16)
    part = part.reshape(n_dp, n_t // 2, 2, mb, tok_dev, rows_p)
    keep = lax.dynamic_index_in_dim(part, my_core, 2, False)
    send = lax.dynamic_index_in_dim(part, 1 - my_core, 2, False)
    recv = lax.ppermute(send, "tensor", [(q, q ^ 1) for q in range(n_t)])
    pair = (keep.astype(jnp.float32) + recv.astype(jnp.float32)).astype(jnp.bfloat16)
    keep = lax.dynamic_index_in_dim(pair, my_hi, 1, False)
    send = lax.dynamic_index_in_dim(pair, 1 - my_hi, 1, False)
    recv = lax.ppermute(send, "tensor", [(q, q ^ 2) for q in range(n_t)])
    total = (keep.astype(jnp.float32) + recv.astype(jnp.float32)).astype(jnp.bfloat16)
    got = lax.all_to_all(total, "dp", 0, 0, tiled=True)
    normed_grad = got.astype(jnp.float32)
    x4 = saved_input[0].reshape(mb, tok_dev, n_dp, rows_p).transpose(2, 0, 1, 3)
    scale4 = inverse_scale[None]
    centered4 = x4.astype(jnp.float32) * scale4
    gain4 = gain_float.reshape(n_dp, 1, 1, rows_p)
    hidden_gradient = normed_grad * gain4
    branch4 = scale4 * (
        hidden_gradient
        - centered4 * jnp.mean(hidden_gradient * centered4, axis=(0, 3), keepdims=True)
    )
    later4 = later_sum(branch4)
    grad_in = (
        top_grad.astype(jnp.float32)
        + (branch4 + later4).transpose(1, 2, 0, 3).reshape(mb, tok_dev, d_model)
    ).astype(jnp.bfloat16)

    own_input, own_gain = lax.optimization_barrier((saved_input[0], norm_gain[0]))
    own_float = own_input.astype(jnp.float32)
    own_scale = lax.rsqrt(jnp.mean(own_float * own_float, axis=-1, keepdims=True) + 1e-05)
    own_normed = ((own_float * own_scale) * own_gain.astype(jnp.float32)).astype(jnp.bfloat16)
    nrm_blocks = own_normed.reshape(mb, tok_dev, n_dp, rows_p)
    pieces = [lax.dynamic_index_in_dim(nrm_blocks, my_p, 2, False)]
    for k in range(1, n_dp):
        send = lax.dynamic_index_in_dim(nrm_blocks, (my_p + k) % n_dp, 2, False)
        pieces.append(
            lax.ppermute(send, "dp", [(q, (q + k) % n_dp) for q in range(n_dp)])
        )
    mine = jnp.stack(pieces)
    far = lax.ppermute(mine, "tensor", [(q, q ^ 2) for q in range(n_t)])
    on_chip = jnp.stack([mine, far])
    hi_order = jnp.where(my_hi == 0, on_chip, on_chip[::-1])
    other = lax.ppermute(hi_order, "tensor", [(q, q ^ 1) for q in range(n_t)])
    both = jnp.where(my_core == 0, jnp.stack([hi_order, other]), jnp.stack([other, hi_order]))
    nrm = both.transpose(1, 0, 2, 3, 4, 5).reshape((n_t,) + mine.shape)
    cot_sel = kv_sel.reshape(n_dp, mb, n_t, tok_dev, width_t).transpose(1, 0, 2, 3, 4)
    groups = (my_p - jnp.arange(n_dp, dtype=jnp.int32)) % n_dp

    row_ids = my_p * jnp.int32(rows_p) + jnp.arange(rows_p, dtype=jnp.int32)
    index = (
        row_ids[:, None] * jnp.int32(total_cols)
        + my_t * jnp.int32(width_t)
        + jnp.arange(width_t, dtype=jnp.int32)[None, :]
    )
    terms = jnp.einsum("tkmid,mktic->kdc", nrm, cot_sel, preferred_element_type=jnp.float32)
    rounded = dither(terms, salt, counter, layer, groups[:, None, None], index[None])
    wsum = jnp.sum(rounded, axis=0)
    return (grad_in[None], wsum[None])


def solution(mesh):
    placed = (
        P("section", None, ("dp", "tensor"), None),
        P("section", None, "dp", "tensor"),
        P("section", "dp", "tensor"),
        P("section", None),
        P(None, ("dp", "tensor"), None),
        P(),
        P(),
    )
    return jax.shard_map(
        body,
        mesh=mesh,
        in_specs=placed,
        out_specs=(P("section", None, ("dp", "tensor"), None), P("section", "dp", "tensor")),
        check_vma=False,
    )
```

```python
import jax
import jax.numpy as jnp
from jax import lax
from jax.sharding import PartitionSpec as P


def mix_bits(salt, counter, layer, group, index):
    h = (
        index * jnp.int32(-1640531535)
        + salt * jnp.int32(374761393)
        + counter * jnp.int32(668265263)
    )
    h = h + layer * jnp.int32(-1028477379) + group * jnp.int32(1274126177)
    h = h ^ lax.shift_right_logical(h, jnp.int32(16))
    h = h * jnp.int32(2146121005)
    h = h ^ lax.shift_right_logical(h, jnp.int32(15))
    h = h * jnp.int32(-2073254261)
    h = h ^ lax.shift_right_logical(h, jnp.int32(16))
    return lax.shift_right_logical(h, jnp.int32(8)).astype(jnp.float32) * (1.0 / 16777216.0)


def dither(term, salt, counter, layer, group, index):
    noise = mix_bits(salt, counter, layer, group, index)
    moved = term * (1.0 + (noise - 0.5) * 0.5)
    return lax.optimization_barrier(moved.astype(jnp.bfloat16)).astype(jnp.float32)


def later_sum(branch4):
    n_sec = lax.axis_size("section")
    chunks = branch4.astype(jnp.bfloat16).reshape(n_sec, -1, branch4.shape[-1])
    got = lax.all_to_all(chunks, "section", 0, 0, tiled=True)
    shifted = jnp.concatenate([got[1:], jnp.zeros_like(got[:1])], axis=0)
    suffix = lax.cumsum(shifted.astype(jnp.float32), axis=0, reverse=True)
    back = lax.all_to_all(suffix.astype(jnp.bfloat16), "section", 0, 0, tiled=True)
    return back.reshape(branch4.shape).astype(jnp.float32)


def body(saved_input, kv_grad, kv_weight, norm_gain, top_grad, noise_salt, step_counter):
    salt = noise_salt[0]
    counter = step_counter[0]
    layer = lax.axis_index("section")
    n_dp = lax.axis_size("dp")
    n_t = lax.axis_size("tensor")
    my_p = lax.axis_index("dp")
    my_t = lax.axis_index("tensor")
    my_core = my_t % 2
    my_hi = my_t // 2
    cotan = kv_grad[0]
    weight = kv_weight[0]
    rows_p, width_t = weight.shape
    total_cols = width_t * n_t
    mb, tok_dev, d_model = saved_input.shape[1:]

    input_float = saved_input[0].astype(jnp.float32)
    inverse_scale = lax.rsqrt(jnp.mean(input_float * input_float, axis=-1, keepdims=True) + 1e-05)
    gain_float = norm_gain[0].astype(jnp.float32)

    kv_pieces = [cotan]
    for k in range(1, n_dp):
        kv_pieces.append(
            lax.ppermute(cotan, "dp", [(q, (q + k) % n_dp) for q in range(n_dp)])
        )
    kv_sel = jnp.stack(kv_pieces)
    kv_rev = jnp.concatenate([kv_sel[::-1], kv_sel[::-1]], axis=0)
    cotan_all = lax.dynamic_slice_in_dim(kv_rev, n_dp - 1 - my_p, n_dp, axis=0)
    cotan_all = cotan_all.transpose(1, 0, 2, 3).reshape(mb, n_dp * cotan.shape[1], width_t)
    part = jnp.einsum(
        "mjik,dk->jmid",
        cotan_all.reshape(mb, n_dp * n_t, tok_dev, width_t),
        weight,
        preferred_element_type=jnp.float32,
    ).astype(jnp.bfloat16)
    part = part.reshape(n_dp, n_t // 2, 2, mb, tok_dev, rows_p)
    keep = lax.dynamic_index_in_dim(part, my_core, 2, False)
    send = lax.dynamic_index_in_dim(part, 1 - my_core, 2, False)
    recv = lax.ppermute(send, "tensor", [(q, q ^ 1) for q in range(n_t)])
    pair = (keep.astype(jnp.float32) + recv.astype(jnp.float32)).astype(jnp.bfloat16)
    keep = lax.dynamic_index_in_dim(pair, my_hi, 1, False)
    send = lax.dynamic_index_in_dim(pair, 1 - my_hi, 1, False)
    recv = lax.ppermute(send, "tensor", [(q, q ^ 2) for q in range(n_t)])
    total = (keep.astype(jnp.float32) + recv.astype(jnp.float32)).astype(jnp.bfloat16)
    got = lax.all_to_all(total, "dp", 0, 0, tiled=True)
    normed_grad = got.astype(jnp.float32)
    x4 = saved_input[0].reshape(mb, tok_dev, n_dp, rows_p).transpose(2, 0, 1, 3)
    scale4 = inverse_scale[None]
    centered4 = x4.astype(jnp.float32) * scale4
    gain4 = gain_float.reshape(n_dp, 1, 1, rows_p)
    hidden_gradient = normed_grad * gain4
    branch4 = scale4 * (
        hidden_gradient
        - centered4 * jnp.mean(hidden_gradient * centered4, axis=(0, 3), keepdims=True)
    )
    top4 = top_grad.reshape(mb, tok_dev, n_dp, rows_p).transpose(2, 0, 1, 3)
    ahead = lax.optimization_barrier(top4.astype(jnp.float32) + branch4)
    later4 = later_sum(branch4)
    grad4 = (ahead + later4).astype(jnp.bfloat16)
    grad_in = grad4.transpose(1, 2, 0, 3).reshape(mb, tok_dev, d_model)

    own_input, own_gain = lax.optimization_barrier((saved_input[0], norm_gain[0]))
    own_float = own_input.astype(jnp.float32)
    own_scale = lax.rsqrt(jnp.mean(own_float * own_float, axis=-1, keepdims=True) + 1e-05)
    own_normed = ((own_float * own_scale) * own_gain.astype(jnp.float32)).astype(jnp.bfloat16)
    nrm_blocks = own_normed.reshape(mb, tok_dev, n_dp, rows_p)
    pieces = [lax.dynamic_index_in_dim(nrm_blocks, my_p, 2, False)]
    for k in range(1, n_dp):
        send = lax.dynamic_index_in_dim(nrm_blocks, (my_p + k) % n_dp, 2, False)
        pieces.append(
            lax.ppermute(send, "dp", [(q, (q + k) % n_dp) for q in range(n_dp)])
        )
    mine = jnp.stack(pieces)
    far = lax.ppermute(mine, "tensor", [(q, q ^ 2) for q in range(n_t)])
    on_chip = jnp.stack([mine, far])
    hi_order = jnp.where(my_hi == 0, on_chip, on_chip[::-1])
    other = lax.ppermute(hi_order, "tensor", [(q, q ^ 1) for q in range(n_t)])
    both = jnp.where(my_core == 0, jnp.stack([hi_order, other]), jnp.stack([other, hi_order]))
    nrm = both.transpose(1, 0, 2, 3, 4, 5).reshape((n_t,) + mine.shape)
    cot_sel = kv_sel.reshape(n_dp, mb, n_t, tok_dev, width_t).transpose(1, 0, 2, 3, 4)
    groups = (my_p - jnp.arange(n_dp, dtype=jnp.int32)) % n_dp

    row_ids = my_p * jnp.int32(rows_p) + jnp.arange(rows_p, dtype=jnp.int32)
    index = (
        row_ids[:, None] * jnp.int32(total_cols)
        + my_t * jnp.int32(width_t)
        + jnp.arange(width_t, dtype=jnp.int32)[None, :]
    )
    terms = jnp.einsum("tkmid,mktic->kdc", nrm, cot_sel, preferred_element_type=jnp.float32)
    rounded = dither(terms, salt, counter, layer, groups[:, None, None], index[None])
    wsum = jnp.sum(rounded, axis=0)
    return (grad_in[None], wsum[None])


def solution(mesh):
    placed = (
        P("section", None, ("dp", "tensor"), None),
        P("section", None, "dp", "tensor"),
        P("section", "dp", "tensor"),
        P("section", None),
        P(None, ("dp", "tensor"), None),
        P(),
        P(),
    )
    return jax.shard_map(
        body,
        mesh=mesh,
        in_specs=placed,
        out_specs=(P("section", None, ("dp", "tensor"), None), P("section", "dp", "tensor")),
        check_vma=False,
    )
```

```python
import jax
import jax.numpy as jnp
from jax import lax
from jax.sharding import PartitionSpec as P


def mix_bits(salt, counter, layer, group, index):
    h = (
        index * jnp.int32(-1640531535)
        + salt * jnp.int32(374761393)
        + counter * jnp.int32(668265263)
    )
    h = h + layer * jnp.int32(-1028477379) + group * jnp.int32(1274126177)
    h = h ^ lax.shift_right_logical(h, jnp.int32(16))
    h = h * jnp.int32(2146121005)
    h = h ^ lax.shift_right_logical(h, jnp.int32(15))
    h = h * jnp.int32(-2073254261)
    h = h ^ lax.shift_right_logical(h, jnp.int32(16))
    return lax.shift_right_logical(h, jnp.int32(8)).astype(jnp.float32) * (1.0 / 16777216.0)


def dither(term, salt, counter, layer, group, index):
    noise = mix_bits(salt, counter, layer, group, index)
    moved = term * (1.0 + (noise - 0.5) * 0.5)
    return lax.optimization_barrier(moved.astype(jnp.bfloat16)).astype(jnp.float32)


def later_sum(branch4):
    n_sec = lax.axis_size("section")
    chunks = branch4.astype(jnp.bfloat16).reshape(n_sec, -1, branch4.shape[-1])
    got = lax.all_to_all(chunks, "section", 0, 0, tiled=True)
    shifted = jnp.concatenate([got[1:], jnp.zeros_like(got[:1])], axis=0)
    suffix = lax.cumsum(shifted.astype(jnp.float32), axis=0, reverse=True)
    back = lax.all_to_all(suffix.astype(jnp.bfloat16), "section", 0, 0, tiled=True)
    return back.reshape(branch4.shape).astype(jnp.float32)


def body(saved_input, kv_grad, kv_weight, norm_gain, top_grad, noise_salt, step_counter):
    salt = noise_salt[0]
    counter = step_counter[0]
    layer = lax.axis_index("section")
    n_dp = lax.axis_size("dp")
    n_t = lax.axis_size("tensor")
    my_p = lax.axis_index("dp")
    my_t = lax.axis_index("tensor")
    my_core = my_t % 2
    my_hi = my_t // 2
    cotan = kv_grad[0]
    weight = kv_weight[0]
    rows_p, width_t = weight.shape
    total_cols = width_t * n_t
    mb, tok_dev, d_model = saved_input.shape[1:]

    input_float = saved_input[0].astype(jnp.float32)
    inverse_scale = lax.rsqrt(jnp.mean(input_float * input_float, axis=-1, keepdims=True) + 1e-05)
    gain_float = norm_gain[0].astype(jnp.float32)

    kv_pieces = [cotan]
    for k in range(1, n_dp):
        kv_pieces.append(
            lax.ppermute(cotan, "dp", [(q, (q + k) % n_dp) for q in range(n_dp)])
        )
    kv_sel = jnp.stack(kv_pieces)
    kv_rev = jnp.concatenate([kv_sel[::-1], kv_sel[::-1]], axis=0)
    cotan_all = lax.dynamic_slice_in_dim(kv_rev, n_dp - 1 - my_p, n_dp, axis=0)
    cotan_all = cotan_all.transpose(1, 0, 2, 3).reshape(mb, n_dp * cotan.shape[1], width_t)
    cot_blocks = cotan_all.reshape(mb, n_dp, n_t // 2, 2, tok_dev, width_t)

    def part_for(core):
        cot_c = lax.dynamic_index_in_dim(cot_blocks, core, 3, False)
        return jnp.einsum(
            "mpxik,dk->pxmid", cot_c, weight, preferred_element_type=jnp.float32
        ).astype(jnp.bfloat16)

    keep = part_for(my_core)
    send = part_for(1 - my_core)
    recv = lax.ppermute(send, "tensor", [(q, q ^ 1) for q in range(n_t)])
    pair = (keep.astype(jnp.float32) + recv.astype(jnp.float32)).astype(jnp.bfloat16)
    keep = lax.dynamic_index_in_dim(pair, my_hi, 1, False)
    send = lax.dynamic_index_in_dim(pair, 1 - my_hi, 1, False)
    recv = lax.ppermute(send, "tensor", [(q, q ^ 2) for q in range(n_t)])
    total = (keep.astype(jnp.float32) + recv.astype(jnp.float32)).astype(jnp.bfloat16)
    got = lax.all_to_all(total, "dp", 0, 0, tiled=True)
    normed_grad = got.astype(jnp.float32)
    x4 = saved_input[0].reshape(mb, tok_dev, n_dp, rows_p).transpose(2, 0, 1, 3)
    scale4 = inverse_scale[None]
    centered4 = x4.astype(jnp.float32) * scale4
    gain4 = gain_float.reshape(n_dp, 1, 1, rows_p)
    hidden_gradient = normed_grad * gain4
    branch4 = scale4 * (
        hidden_gradient
        - centered4 * jnp.mean(hidden_gradient * centered4, axis=(0, 3), keepdims=True)
    )
    top4 = top_grad.reshape(mb, tok_dev, n_dp, rows_p).transpose(2, 0, 1, 3)
    ahead = lax.optimization_barrier(top4.astype(jnp.float32) + branch4)
    later4 = later_sum(branch4)
    grad4 = (ahead + later4).astype(jnp.bfloat16)
    grad_in = grad4.transpose(1, 2, 0, 3).reshape(mb, tok_dev, d_model)

    own_input, own_gain = lax.optimization_barrier((saved_input[0], norm_gain[0]))
    own_float = own_input.astype(jnp.float32)
    own_scale = lax.rsqrt(jnp.mean(own_float * own_float, axis=-1, keepdims=True) + 1e-05)
    own_normed = ((own_float * own_scale) * own_gain.astype(jnp.float32)).astype(jnp.bfloat16)
    nrm_blocks = own_normed.reshape(mb, tok_dev, n_dp, rows_p)
    pieces = [lax.dynamic_index_in_dim(nrm_blocks, my_p, 2, False)]
    for k in range(1, n_dp):
        send = lax.dynamic_index_in_dim(nrm_blocks, (my_p + k) % n_dp, 2, False)
        pieces.append(
            lax.ppermute(send, "dp", [(q, (q + k) % n_dp) for q in range(n_dp)])
        )
    mine = jnp.stack(pieces)
    far = lax.ppermute(mine, "tensor", [(q, q ^ 2) for q in range(n_t)])
    on_chip = jnp.stack([mine, far])
    hi_order = jnp.where(my_hi == 0, on_chip, on_chip[::-1])
    other = lax.ppermute(hi_order, "tensor", [(q, q ^ 1) for q in range(n_t)])
    both = jnp.where(my_core == 0, jnp.stack([hi_order, other]), jnp.stack([other, hi_order]))
    nrm = both.transpose(1, 0, 2, 3, 4, 5).reshape((n_t,) + mine.shape)
    cot_sel = kv_sel.reshape(n_dp, mb, n_t, tok_dev, width_t).transpose(1, 0, 2, 3, 4)
    groups = (my_p - jnp.arange(n_dp, dtype=jnp.int32)) % n_dp

    row_ids = my_p * jnp.int32(rows_p) + jnp.arange(rows_p, dtype=jnp.int32)
    index = (
        row_ids[:, None] * jnp.int32(total_cols)
        + my_t * jnp.int32(width_t)
        + jnp.arange(width_t, dtype=jnp.int32)[None, :]
    )
    terms = jnp.einsum("tkmid,mktic->kdc", nrm, cot_sel, preferred_element_type=jnp.float32)
    rounded = dither(terms, salt, counter, layer, groups[:, None, None], index[None])
    wsum = jnp.sum(rounded, axis=0)
    return (grad_in[None], wsum[None])


def solution(mesh):
    placed = (
        P("section", None, ("dp", "tensor"), None),
        P("section", None, "dp", "tensor"),
        P("section", "dp", "tensor"),
        P("section", None),
        P(None, ("dp", "tensor"), None),
        P(),
        P(),
    )
    return jax.shard_map(
        body,
        mesh=mesh,
        in_specs=placed,
        out_specs=(P("section", None, ("dp", "tensor"), None), P("section", "dp", "tensor")),
        check_vma=False,
    )
```

```python
import jax
import jax.numpy as jnp
from jax import lax
from jax.sharding import PartitionSpec as P


def mix_bits(salt, counter, layer, group, index):
    h = (
        index * jnp.int32(-1640531535)
        + salt * jnp.int32(374761393)
        + counter * jnp.int32(668265263)
    )
    h = h + layer * jnp.int32(-1028477379) + group * jnp.int32(1274126177)
    h = h ^ lax.shift_right_logical(h, jnp.int32(16))
    h = h * jnp.int32(2146121005)
    h = h ^ lax.shift_right_logical(h, jnp.int32(15))
    h = h * jnp.int32(-2073254261)
    h = h ^ lax.shift_right_logical(h, jnp.int32(16))
    return lax.shift_right_logical(h, jnp.int32(8)).astype(jnp.float32) * (1.0 / 16777216.0)


def dither(term, salt, counter, layer, group, index):
    noise = mix_bits(salt, counter, layer, group, index)
    moved = term * (1.0 + (noise - 0.5) * 0.5)
    return lax.optimization_barrier(moved.astype(jnp.bfloat16)).astype(jnp.float32)


def later_sum(branch4):
    n_sec = lax.axis_size("section")
    chunks = branch4.astype(jnp.bfloat16).reshape(n_sec, -1, branch4.shape[-1])
    got = lax.all_to_all(chunks, "section", 0, 0, tiled=True)
    shifted = jnp.concatenate([got[1:], jnp.zeros_like(got[:1])], axis=0)
    suffix = lax.cumsum(shifted.astype(jnp.float32), axis=0, reverse=True)
    back = lax.all_to_all(suffix.astype(jnp.bfloat16), "section", 0, 0, tiled=True)
    return back.reshape(branch4.shape).astype(jnp.float32)


def body(saved_input, kv_grad, kv_weight, norm_gain, top_grad, noise_salt, step_counter):
    salt = noise_salt[0]
    counter = step_counter[0]
    layer = lax.axis_index("section")
    n_dp = lax.axis_size("dp")
    n_t = lax.axis_size("tensor")
    my_p = lax.axis_index("dp")
    my_t = lax.axis_index("tensor")
    my_core = my_t % 2
    my_hi = my_t // 2
    cotan = kv_grad[0]
    weight = kv_weight[0]
    rows_p, width_t = weight.shape
    total_cols = width_t * n_t
    mb, tok_dev, d_model = saved_input.shape[1:]

    input_float = saved_input[0].astype(jnp.float32)
    inverse_scale = lax.rsqrt(jnp.mean(input_float * input_float, axis=-1, keepdims=True) + 1e-05)
    gain_float = norm_gain[0].astype(jnp.float32)

    kv_pieces = [cotan]
    for k in range(1, n_dp):
        kv_pieces.append(
            lax.ppermute(cotan, "dp", [(q, (q + k) % n_dp) for q in range(n_dp)])
        )
    kv_sel = jnp.stack(kv_pieces)
    blocks = []
    for j in range(n_dp):
        pick = kv_pieces[0]
        for k in range(1, n_dp):
            pick = jnp.where((my_p - k) % n_dp == j, kv_pieces[k], pick)
        blocks.append(pick)
    cotan_all = jnp.concatenate(blocks, axis=1)
    cot_blocks = cotan_all.reshape(mb, n_dp, n_t // 2, 2, tok_dev, width_t)

    def part_for(core):
        cot_c = lax.dynamic_index_in_dim(cot_blocks, core, 3, False)
        return jnp.einsum(
            "mpxik,dk->pxmid", cot_c, weight, preferred_element_type=jnp.float32
        ).astype(jnp.bfloat16)

    keep = part_for(my_core)
    send = part_for(1 - my_core)
    recv = lax.ppermute(send, "tensor", [(q, q ^ 1) for q in range(n_t)])
    pair = (keep.astype(jnp.float32) + recv.astype(jnp.float32)).astype(jnp.bfloat16)
    keep = lax.dynamic_index_in_dim(pair, my_hi, 1, False)
    send = lax.dynamic_index_in_dim(pair, 1 - my_hi, 1, False)
    recv = lax.ppermute(send, "tensor", [(q, q ^ 2) for q in range(n_t)])
    total = (keep.astype(jnp.float32) + recv.astype(jnp.float32)).astype(jnp.bfloat16)
    got = lax.all_to_all(total, "dp", 0, 0, tiled=True)
    normed_grad = got.astype(jnp.float32)
    x4 = saved_input[0].reshape(mb, tok_dev, n_dp, rows_p).transpose(2, 0, 1, 3)
    scale4 = inverse_scale[None]
    centered4 = x4.astype(jnp.float32) * scale4
    gain4 = gain_float.reshape(n_dp, 1, 1, rows_p)
    hidden_gradient = normed_grad * gain4
    branch4 = scale4 * (
        hidden_gradient
        - centered4 * jnp.mean(hidden_gradient * centered4, axis=(0, 3), keepdims=True)
    )
    top4 = top_grad.reshape(mb, tok_dev, n_dp, rows_p).transpose(2, 0, 1, 3)
    ahead = lax.optimization_barrier(top4.astype(jnp.float32) + branch4)
    later4 = later_sum(branch4)
    grad4 = (ahead + later4).astype(jnp.bfloat16)
    grad_in = grad4.transpose(1, 2, 0, 3).reshape(mb, tok_dev, d_model)

    own_input, own_gain = lax.optimization_barrier((saved_input[0], norm_gain[0]))
    own_float = own_input.astype(jnp.float32)
    own_scale = lax.rsqrt(jnp.mean(own_float * own_float, axis=-1, keepdims=True) + 1e-05)
    own_normed = ((own_float * own_scale) * own_gain.astype(jnp.float32)).astype(jnp.bfloat16)
    nrm_blocks = own_normed.reshape(mb, tok_dev, n_dp, rows_p)
    pieces = [lax.dynamic_index_in_dim(nrm_blocks, my_p, 2, False)]
    for k in range(1, n_dp):
        send = lax.dynamic_index_in_dim(nrm_blocks, (my_p + k) % n_dp, 2, False)
        pieces.append(
            lax.ppermute(send, "dp", [(q, (q + k) % n_dp) for q in range(n_dp)])
        )
    mine = jnp.stack(pieces)
    far = lax.ppermute(mine, "tensor", [(q, q ^ 2) for q in range(n_t)])
    on_chip = jnp.stack([mine, far])
    hi_order = jnp.where(my_hi == 0, on_chip, on_chip[::-1])
    other = lax.ppermute(hi_order, "tensor", [(q, q ^ 1) for q in range(n_t)])
    both = jnp.where(my_core == 0, jnp.stack([hi_order, other]), jnp.stack([other, hi_order]))
    nrm = both.transpose(1, 0, 2, 3, 4, 5).reshape((n_t,) + mine.shape)
    cot_sel = kv_sel.reshape(n_dp, mb, n_t, tok_dev, width_t).transpose(1, 0, 2, 3, 4)
    groups = (my_p - jnp.arange(n_dp, dtype=jnp.int32)) % n_dp

    row_ids = my_p * jnp.int32(rows_p) + jnp.arange(rows_p, dtype=jnp.int32)
    index = (
        row_ids[:, None] * jnp.int32(total_cols)
        + my_t * jnp.int32(width_t)
        + jnp.arange(width_t, dtype=jnp.int32)[None, :]
    )
    terms = jnp.einsum("tkmid,mktic->kdc", nrm, cot_sel, preferred_element_type=jnp.float32)
    rounded = dither(terms, salt, counter, layer, groups[:, None, None], index[None])
    wsum = jnp.sum(rounded, axis=0)
    return (grad_in[None], wsum[None])


def solution(mesh):
    placed = (
        P("section", None, ("dp", "tensor"), None),
        P("section", None, "dp", "tensor"),
        P("section", "dp", "tensor"),
        P("section", None),
        P(None, ("dp", "tensor"), None),
        P(),
        P(),
    )
    return jax.shard_map(
        body,
        mesh=mesh,
        in_specs=placed,
        out_specs=(P("section", None, ("dp", "tensor"), None), P("section", "dp", "tensor")),
        check_vma=False,
    )
```

```python
import jax
import jax.numpy as jnp
from jax import lax
from jax.sharding import PartitionSpec as P


def mix_bits(salt, counter, layer, group, index):
    h = (
        index * jnp.int32(-1640531535)
        + salt * jnp.int32(374761393)
        + counter * jnp.int32(668265263)
    )
    h = h + layer * jnp.int32(-1028477379) + group * jnp.int32(1274126177)
    h = h ^ lax.shift_right_logical(h, jnp.int32(16))
    h = h * jnp.int32(2146121005)
    h = h ^ lax.shift_right_logical(h, jnp.int32(15))
    h = h * jnp.int32(-2073254261)
    h = h ^ lax.shift_right_logical(h, jnp.int32(16))
    return lax.shift_right_logical(h, jnp.int32(8)).astype(jnp.float32) * (1.0 / 16777216.0)


def dither(term, salt, counter, layer, group, index):
    noise = mix_bits(salt, counter, layer, group, index)
    moved = term * (1.0 + (noise - 0.5) * 0.5)
    return lax.optimization_barrier(moved.astype(jnp.bfloat16)).astype(jnp.float32)


def later_sum(branch4):
    n_sec = lax.axis_size("section")
    chunks = branch4.astype(jnp.bfloat16).reshape(n_sec, -1, branch4.shape[-1])
    got = lax.all_to_all(chunks, "section", 0, 0, tiled=True)
    shifted = jnp.concatenate([got[1:], jnp.zeros_like(got[:1])], axis=0)
    suffix = lax.cumsum(shifted.astype(jnp.float32), axis=0, reverse=True)
    back = lax.all_to_all(suffix.astype(jnp.bfloat16), "section", 0, 0, tiled=True)
    return back.reshape(branch4.shape).astype(jnp.float32)


def body(saved_input, kv_grad, kv_weight, norm_gain, top_grad, noise_salt, step_counter):
    salt = noise_salt[0]
    counter = step_counter[0]
    layer = lax.axis_index("section")
    n_dp = lax.axis_size("dp")
    n_t = lax.axis_size("tensor")
    my_p = lax.axis_index("dp")
    my_t = lax.axis_index("tensor")
    my_core = my_t % 2
    my_hi = my_t // 2
    cotan = kv_grad[0]
    weight = kv_weight[0]
    rows_p, width_t = weight.shape
    total_cols = width_t * n_t
    mb, tok_dev, d_model = saved_input.shape[1:]

    input_float = saved_input[0].astype(jnp.float32)
    inverse_scale = lax.rsqrt(jnp.mean(input_float * input_float, axis=-1, keepdims=True) + 1e-05)
    gain_float = norm_gain[0].astype(jnp.float32)

    kv_pieces = [cotan]
    for k in range(1, n_dp):
        kv_pieces.append(
            lax.ppermute(cotan, "dp", [(q, (q + k) % n_dp) for q in range(n_dp)])
        )
    kv_sel = jnp.stack(kv_pieces)
    blocks = []
    for j in range(n_dp):
        pick = kv_pieces[0]
        for k in range(1, n_dp):
            pick = jnp.where((my_p - k) % n_dp == j, kv_pieces[k], pick)
        blocks.append(pick)
    cotan_all = jnp.concatenate(blocks, axis=1)
    cot_blocks = cotan_all.reshape(mb, n_dp, n_t // 2, 2, tok_dev, width_t)

    def part_for(core):
        cot_c = lax.dynamic_index_in_dim(cot_blocks, core, 3, False)
        return jnp.einsum(
            "mpxik,dk->pxmid", cot_c, weight, preferred_element_type=jnp.float32
        ).astype(jnp.bfloat16)

    keep = part_for(my_core)
    send = part_for(1 - my_core)
    recv = lax.ppermute(send, "tensor", [(q, q ^ 1) for q in range(n_t)])
    pair = (keep.astype(jnp.float32) + recv.astype(jnp.float32)).astype(jnp.bfloat16)
    keep = lax.dynamic_index_in_dim(pair, my_hi, 1, False)
    send = lax.dynamic_index_in_dim(pair, 1 - my_hi, 1, False)
    recv = lax.ppermute(send, "tensor", [(q, q ^ 2) for q in range(n_t)])
    total = (keep.astype(jnp.float32) + recv.astype(jnp.float32)).astype(jnp.bfloat16)
    got = lax.all_to_all(total, "dp", 0, 0, tiled=True)
    normed_grad = got.astype(jnp.float32)
    x4 = saved_input[0].reshape(mb, tok_dev, n_dp, rows_p).transpose(2, 0, 1, 3)
    scale4 = inverse_scale[None]
    centered4 = x4.astype(jnp.float32) * scale4
    gain4 = gain_float.reshape(n_dp, 1, 1, rows_p)
    hidden_gradient = normed_grad * gain4
    branch4 = scale4 * (
        hidden_gradient
        - centered4 * jnp.mean(hidden_gradient * centered4, axis=(0, 3), keepdims=True)
    )

    def out_layout(v):
        return v.transpose(1, 2, 0, 3).reshape(mb, tok_dev, d_model)

    ahead = lax.optimization_barrier(top_grad.astype(jnp.float32) + out_layout(branch4))
    later4 = later_sum(branch4)
    grad_in = (ahead + out_layout(later4)).astype(jnp.bfloat16)

    own_input, own_gain = lax.optimization_barrier((saved_input[0], norm_gain[0]))
    own_float = own_input.astype(jnp.float32)
    own_scale = lax.rsqrt(jnp.mean(own_float * own_float, axis=-1, keepdims=True) + 1e-05)
    own_normed = ((own_float * own_scale) * own_gain.astype(jnp.float32)).astype(jnp.bfloat16)
    nrm_blocks = own_normed.reshape(mb, tok_dev, n_dp, rows_p)
    pieces = [lax.dynamic_index_in_dim(nrm_blocks, my_p, 2, False)]
    for k in range(1, n_dp):
        send = lax.dynamic_index_in_dim(nrm_blocks, (my_p + k) % n_dp, 2, False)
        pieces.append(
            lax.ppermute(send, "dp", [(q, (q + k) % n_dp) for q in range(n_dp)])
        )
    mine = jnp.stack(pieces)
    far = lax.ppermute(mine, "tensor", [(q, q ^ 2) for q in range(n_t)])
    on_chip = jnp.stack([mine, far])
    hi_order = jnp.where(my_hi == 0, on_chip, on_chip[::-1])
    other = lax.ppermute(hi_order, "tensor", [(q, q ^ 1) for q in range(n_t)])
    both = jnp.where(my_core == 0, jnp.stack([hi_order, other]), jnp.stack([other, hi_order]))
    nrm = both.transpose(1, 0, 2, 3, 4, 5).reshape((n_t,) + mine.shape)
    cot_sel = kv_sel.reshape(n_dp, mb, n_t, tok_dev, width_t).transpose(1, 0, 2, 3, 4)
    groups = (my_p - jnp.arange(n_dp, dtype=jnp.int32)) % n_dp

    row_ids = my_p * jnp.int32(rows_p) + jnp.arange(rows_p, dtype=jnp.int32)
    index = (
        row_ids[:, None] * jnp.int32(total_cols)
        + my_t * jnp.int32(width_t)
        + jnp.arange(width_t, dtype=jnp.int32)[None, :]
    )
    terms = jnp.einsum("tkmid,mktic->kdc", nrm, cot_sel, preferred_element_type=jnp.float32)
    rounded = dither(terms, salt, counter, layer, groups[:, None, None], index[None])
    wsum = jnp.sum(rounded, axis=0)
    return (grad_in[None], wsum[None])


def solution(mesh):
    placed = (
        P("section", None, ("dp", "tensor"), None),
        P("section", None, "dp", "tensor"),
        P("section", "dp", "tensor"),
        P("section", None),
        P(None, ("dp", "tensor"), None),
        P(),
        P(),
    )
    return jax.shard_map(
        body,
        mesh=mesh,
        in_specs=placed,
        out_specs=(P("section", None, ("dp", "tensor"), None), P("section", "dp", "tensor")),
        check_vma=False,
    )
```

```python
import jax
import jax.numpy as jnp
from jax import lax
from jax.sharding import PartitionSpec as P


def mix_bits(salt, counter, layer, group, index):
    h = (
        index * jnp.int32(-1640531535)
        + salt * jnp.int32(374761393)
        + counter * jnp.int32(668265263)
    )
    h = h + layer * jnp.int32(-1028477379) + group * jnp.int32(1274126177)
    h = h ^ lax.shift_right_logical(h, jnp.int32(16))
    h = h * jnp.int32(2146121005)
    h = h ^ lax.shift_right_logical(h, jnp.int32(15))
    h = h * jnp.int32(-2073254261)
    h = h ^ lax.shift_right_logical(h, jnp.int32(16))
    return lax.shift_right_logical(h, jnp.int32(8)).astype(jnp.float32) * (1.0 / 16777216.0)


def dither(term, salt, counter, layer, group, index):
    noise = mix_bits(salt, counter, layer, group, index)
    moved = term * (1.0 + (noise - 0.5) * 0.5)
    return lax.optimization_barrier(moved.astype(jnp.bfloat16)).astype(jnp.float32)


def later_sum(branch4):
    n_sec = lax.axis_size("section")
    chunks = branch4.astype(jnp.bfloat16).reshape(n_sec, -1, branch4.shape[-1])
    got = lax.all_to_all(chunks, "section", 0, 0, tiled=True)
    shifted = jnp.concatenate([got[1:], jnp.zeros_like(got[:1])], axis=0)
    suffix = lax.cumsum(shifted.astype(jnp.float32), axis=0, reverse=True)
    back = lax.all_to_all(suffix.astype(jnp.bfloat16), "section", 0, 0, tiled=True)
    return back.reshape(branch4.shape).astype(jnp.float32)


def body(saved_input, kv_grad, kv_weight, norm_gain, top_grad, noise_salt, step_counter):
    salt = noise_salt[0]
    counter = step_counter[0]
    layer = lax.axis_index("section")
    n_dp = lax.axis_size("dp")
    n_t = lax.axis_size("tensor")
    my_p = lax.axis_index("dp")
    my_t = lax.axis_index("tensor")
    my_core = my_t % 2
    my_hi = my_t // 2
    cotan = kv_grad[0]
    weight = kv_weight[0]
    rows_p, width_t = weight.shape
    total_cols = width_t * n_t
    mb, tok_dev, d_model = saved_input.shape[1:]

    input_float = saved_input[0].astype(jnp.float32)
    inverse_scale = lax.rsqrt(jnp.mean(input_float * input_float, axis=-1, keepdims=True) + 1e-05)
    gain_float = norm_gain[0].astype(jnp.float32)

    kv_pieces = [cotan]
    for k in range(1, n_dp):
        kv_pieces.append(
            lax.ppermute(cotan, "dp", [(q, (q + k) % n_dp) for q in range(n_dp)])
        )
    kv_sel = jnp.stack(kv_pieces)
    blocks = []
    for j in range(n_dp):
        pick = kv_pieces[0]
        for k in range(1, n_dp):
            pick = jnp.where((my_p - k) % n_dp == j, kv_pieces[k], pick)
        blocks.append(pick)
    cotan_all = jnp.concatenate(blocks, axis=1)
    cot_blocks = cotan_all.reshape(mb, n_dp, n_t // 2, 2, tok_dev, width_t)

    def part_for(core):
        cot_c = lax.dynamic_index_in_dim(cot_blocks, core, 3, False)
        return jnp.einsum(
            "mpxik,dk->pxmid", cot_c, weight, preferred_element_type=jnp.float32
        ).astype(jnp.bfloat16)

    keep = part_for(my_core)
    send = part_for(1 - my_core)
    recv = lax.ppermute(send, "tensor", [(q, q ^ 1) for q in range(n_t)])

    def pair_half(hi):
        a = lax.dynamic_index_in_dim(keep, hi, 1, False).astype(jnp.float32)
        b = lax.dynamic_index_in_dim(recv, hi, 1, False).astype(jnp.float32)
        return (a + b).astype(jnp.bfloat16)

    keep, send = pair_half(my_hi), pair_half(1 - my_hi)
    recv = lax.ppermute(send, "tensor", [(q, q ^ 2) for q in range(n_t)])
    total = (keep.astype(jnp.float32) + recv.astype(jnp.float32)).astype(jnp.bfloat16)
    got = lax.all_to_all(total, "dp", 0, 0, tiled=True)
    normed_grad = got.astype(jnp.float32)
    x4 = saved_input[0].reshape(mb, tok_dev, n_dp, rows_p).transpose(2, 0, 1, 3)
    scale4 = inverse_scale[None]
    centered4 = x4.astype(jnp.float32) * scale4
    gain4 = gain_float.reshape(n_dp, 1, 1, rows_p)
    hidden_gradient = normed_grad * gain4
    branch4 = scale4 * (
        hidden_gradient
        - centered4 * jnp.mean(hidden_gradient * centered4, axis=(0, 3), keepdims=True)
    )

    def out_layout(v):
        return v.transpose(1, 2, 0, 3).reshape(mb, tok_dev, d_model)

    ahead = lax.optimization_barrier(top_grad.astype(jnp.float32) + out_layout(branch4))
    later4 = later_sum(branch4)
    grad_in = (ahead + out_layout(later4)).astype(jnp.bfloat16)

    own_input, own_gain = lax.optimization_barrier((saved_input[0], norm_gain[0]))
    own_float = own_input.astype(jnp.float32)
    own_scale = lax.rsqrt(jnp.mean(own_float * own_float, axis=-1, keepdims=True) + 1e-05)
    own_normed = ((own_float * own_scale) * own_gain.astype(jnp.float32)).astype(jnp.bfloat16)
    nrm_blocks = own_normed.reshape(mb, tok_dev, n_dp, rows_p)
    pieces = [lax.dynamic_index_in_dim(nrm_blocks, my_p, 2, False)]
    for k in range(1, n_dp):
        send = lax.dynamic_index_in_dim(nrm_blocks, (my_p + k) % n_dp, 2, False)
        pieces.append(
            lax.ppermute(send, "dp", [(q, (q + k) % n_dp) for q in range(n_dp)])
        )
    mine = jnp.stack(pieces)
    far = lax.ppermute(mine, "tensor", [(q, q ^ 2) for q in range(n_t)])
    on_chip = jnp.stack([mine, far])
    hi_order = jnp.where(my_hi == 0, on_chip, on_chip[::-1])
    other = lax.ppermute(hi_order, "tensor", [(q, q ^ 1) for q in range(n_t)])
    both = jnp.where(my_core == 0, jnp.stack([hi_order, other]), jnp.stack([other, hi_order]))
    nrm = both.transpose(1, 0, 2, 3, 4, 5).reshape((n_t,) + mine.shape)
    cot_sel = kv_sel.reshape(n_dp, mb, n_t, tok_dev, width_t).transpose(1, 0, 2, 3, 4)
    groups = (my_p - jnp.arange(n_dp, dtype=jnp.int32)) % n_dp

    row_ids = my_p * jnp.int32(rows_p) + jnp.arange(rows_p, dtype=jnp.int32)
    index = (
        row_ids[:, None] * jnp.int32(total_cols)
        + my_t * jnp.int32(width_t)
        + jnp.arange(width_t, dtype=jnp.int32)[None, :]
    )
    terms = jnp.einsum("tkmid,mktic->kdc", nrm, cot_sel, preferred_element_type=jnp.float32)
    rounded = dither(terms, salt, counter, layer, groups[:, None, None], index[None])
    wsum = jnp.sum(rounded, axis=0)
    return (grad_in[None], wsum[None])


def solution(mesh):
    placed = (
        P("section", None, ("dp", "tensor"), None),
        P("section", None, "dp", "tensor"),
        P("section", "dp", "tensor"),
        P("section", None),
        P(None, ("dp", "tensor"), None),
        P(),
        P(),
    )
    return jax.shard_map(
        body,
        mesh=mesh,
        in_specs=placed,
        out_specs=(P("section", None, ("dp", "tensor"), None), P("section", "dp", "tensor")),
        check_vma=False,
    )
```
